32 devices in a mesh: dp: 8 (over y, x, core), tensor: 4 (over z).
Axes of the slice: x: 2, y: 2, z: 4, core: 2. Of those that a mesh axis runs over, the one named last changes fastest.
Arguments:
- grad_out: bfloat16 [2048, 4096], P('dp'), may hold values from -1.5 to 1.5
- gate_input: bfloat16 [2048, 14336], P('dp', 'tensor'), may hold values from -6 to 6
- up_input: bfloat16 [2048, 14336], P('dp', 'tensor'), may hold values from -6 to 6
- next_hidden: bfloat16 [2048, 14336], P('dp', 'tensor'), may hold values from -6 to 6
- down_weight: bfloat16 [4096, 14336], P(None, 'tensor'), may hold values from -0.046875 to 0.046875
- first_moment: float32 [4096, 14336], P('dp', 'tensor'), may hold values from -48 to 48
- second_moment: float32 [4096, 14336], P('dp', 'tensor'), may hold values from 10 to 200
Outputs:
- gate_grad: bfloat16 [2048, 14336], P('dp', 'tensor')
- up_grad: bfloat16 [2048, 14336], P('dp', 'tensor')
- moment_one: float32 [4096, 14336], P('dp', 'tensor')
- moment_two: float32 [4096, 14336], P('dp', 'tensor')
- next_out: bfloat16 [2048, 4096], P('dp', 'tensor')
The draws below stay inside these ranges and needn't reach their ends.
All inputs are finite; a program needn't handle non-finite values.
Results may differ from the reference program's by a relative error of at most 0.004.
The reference program's roundings to bfloat16 on the way (of `hidden` and `new_weight`) count: a program that leaves them out, or rounds other values in their place, can miss the bound.
Values may be sent and summed in bfloat16 or wider, within the bound.
No kernel may reach another device: no remote copies, remote signals or barrier semaphores. Data moves between devices by JAX's collectives and lax.ppermute only.
A program may use at most 256 MiB of HBM per device.

```python
import math
import jax
import jax.numpy as jnp
from jax import lax

D = 4096
FF = 14336
TOK_DEV = 256
STEP = 20
TOKENS = 2048
N_DP = 8


def with_spikes(result, own_key, source, target, blocks, factor):
    def block_of(dim):
        return (jnp.arange(result.shape[dim]) // (result.shape[dim] // blocks)).reshape((-1,) + (1,) * (result.ndim - 1 - dim))

    one_side = jax.random.permutation(own_key, blocks)[block_of(target)]
    second = (block_of(target) + blocks // 2) % blocks
    return jnp.where((block_of(source) == one_side) | (block_of(source) == second), factor * result, result)


def block_scale(own_key, dims, pieces, low, high):
    def one(position, blocks):
        draws = jax.random.uniform(jax.random.fold_in(jax.random.fold_in(own_key, 6), position), (blocks,), jnp.float32, low / len(pieces), high / len(pieces))
        return jnp.repeat(jnp.exp(draws), dims[position] // blocks).reshape((-1,) + (1,) * (len(dims) - position - 1))

    gain = one(*pieces[0])
    for cut in pieces[1:]:
        gain = gain * one(*cut)
    return gain


def noise(rng, extent, deviation, limit, cuts=(), kind=jnp.bfloat16):
    loudness = block_scale(rng, extent, cuts, -0.22, 0.18) if cuts else 1.0
    entries = jax.random.normal(rng, extent, jnp.float32) * deviation * loudness
    return jnp.minimum(jnp.maximum(entries, -limit), limit).astype(kind)


def gaussian_with(key, shape, deviation, reach, cuts, heavy, dtype=jnp.bfloat16):
    entries = deviation * jax.random.normal(key, shape, jnp.float32)
    if cuts:
        entries = entries * block_scale(key, shape, cuts, -0.22, 0.18)
    return jnp.clip(with_spikes(entries, jax.random.fold_in(key, 3), *heavy), -reach, reach).astype(dtype)


def setup_inputs(seed: int = 0) -> dict:
    keys = jax.random.split(jax.random.key(seed), 8)
    return {
        "grad_out": gaussian_with(keys[0], (TOKENS, D), 0.25, 1.5, ((0, 8),), (0, 1, 8, 2.0)),
        "gate_input": noise(keys[1], (TOKENS, FF), 1.0, 6.0, ((0, 8), (1, 4))),
        "up_input": noise(keys[2], (TOKENS, FF), 1.0, 6.0, ((0, 8), (1, 4))),
        "next_hidden": noise(keys[3], (TOKENS, FF), 1.0, 6.0, ((0, 8), (1, 4))),
        "down_weight": noise(keys[4], (D, FF), FF ** -0.5, 0.046875, ((1, 4),)),
        "first_moment": noise(keys[5], (D, FF), 8.0, 48.0, ((0, 8), (1, 4)), jnp.float32),
        "second_moment": jnp.clip(jnp.exp(math.log(200.0) - 2.9957323 * jax.random.uniform(keys[6], (D, FF), jnp.float32) ** block_scale(keys[6], (D, FF), ((0, 8), (1, 4)), -0.2, 0.2)), 10.0, 200.0),
    }


beta_one = 0.9
beta_two = 0.95
learn_rate = 0.001
decay_rate = 0.1
epsilon = 1e-08

def reference(grad_out, gate_input, up_input, next_hidden, down_weight, first_moment, second_moment):
    gate_value = gate_input.astype(jnp.float32)
    up_value = up_input.astype(jnp.float32)
    sigmoid_gate = jax.nn.sigmoid(gate_value)
    activated = gate_value * sigmoid_gate
    hidden = (activated * up_value).astype(jnp.bfloat16)
    grad_hidden = jnp.dot(grad_out, down_weight, preferred_element_type=jnp.float32)
    gate_grad = (grad_hidden * up_value * sigmoid_gate * (1.0 + gate_value * (1.0 - sigmoid_gate))).astype(jnp.bfloat16)
    up_grad = (grad_hidden * activated).astype(jnp.bfloat16)
    grad_blocks = grad_out.reshape(N_DP, TOK_DEV, D)
    hidden_blocks = hidden.reshape(N_DP, TOK_DEV, FF)

    def add_block(total, pair):
        partial_sum = jnp.dot(pair[0].T, pair[1], preferred_element_type=jnp.float32).astype(jnp.bfloat16)
        partial_sum = lax.optimization_barrier(partial_sum)
        return (total + partial_sum.astype(jnp.float32), None)
    weight_grad, _ = lax.scan(add_block, jnp.zeros((D, FF), jnp.float32), (grad_blocks, hidden_blocks))
    moment_one = beta_one * first_moment + (1.0 - beta_one) * weight_grad
    moment_two = beta_two * second_moment + (1.0 - beta_two) * weight_grad * weight_grad
    corrected_one = moment_one / (1.0 - beta_one ** STEP)
    corrected_two = moment_two / (1.0 - beta_two ** STEP)
    old_weight = down_weight.astype(jnp.float32)
    new_weight = (old_weight - learn_rate * (corrected_one / (jnp.sqrt(corrected_two) + epsilon) + decay_rate * old_weight)).astype(jnp.bfloat16)
    next_out = jnp.dot(next_hidden, new_weight.T, preferred_element_type=jnp.float32).astype(jnp.bfloat16)
    return (gate_grad, up_grad, moment_one, moment_two, next_out)
```

```python
import jax
import jax.numpy as jnp
from jax import lax
from jax.sharding import PartitionSpec as P

STEP = 20


beta_one = 0.9
beta_two = 0.95
learn_rate = 0.001
decay_rate = 0.1
epsilon = 1e-08


def shards(grad_out, gate_input, up_input, next_hidden, down_weight, first_moment, second_moment):
    n_dp = lax.axis_size("dp")
    n_t = lax.axis_size("tensor")
    me = lax.axis_index("dp")
    col = lax.axis_index("tensor")
    tok = grad_out.shape[0]
    owned_rows = first_moment.shape[0]
    group = n_dp // n_t

    gate_value = gate_input.astype(jnp.float32)
    up_value = up_input.astype(jnp.float32)
    sigmoid_gate = jax.nn.sigmoid(gate_value)
    activated = gate_value * sigmoid_gate
    hidden = (activated * up_value).astype(jnp.bfloat16)

    hidden_all = lax.all_gather(hidden, "dp", axis=0, tiled=True)
    next_all = lax.all_gather(next_hidden, "dp", axis=0, tiled=True)
    grad_rows = lax.all_to_all(grad_out, "dp", 1, 0, tiled=True)

    grad_hidden = jnp.dot(grad_out, down_weight, preferred_element_type=jnp.float32)
    gate_grad = (
        grad_hidden * up_value * sigmoid_gate * (1.0 + gate_value * (1.0 - sigmoid_gate))
    ).astype(jnp.bfloat16)
    up_grad = (grad_hidden * activated).astype(jnp.bfloat16)

    weight_grad = jnp.zeros((owned_rows, hidden.shape[1]), jnp.float32)
    for b in range(n_dp):
        block = lax.dot_general(
            grad_rows[b * tok : (b + 1) * tok],
            hidden_all[b * tok : (b + 1) * tok],
            (((0,), (0,)), ((), ())),
            preferred_element_type=jnp.float32,
        ).astype(jnp.bfloat16)
        weight_grad = weight_grad + block.astype(jnp.float32)

    moment_one = beta_one * first_moment + (1.0 - beta_one) * weight_grad
    moment_two = beta_two * second_moment + (1.0 - beta_two) * weight_grad * weight_grad
    corrected_one = moment_one / (1.0 - beta_one**STEP)
    corrected_two = moment_two / (1.0 - beta_two**STEP)
    old_shard = lax.dynamic_slice_in_dim(down_weight, me * owned_rows, owned_rows, 0).astype(
        jnp.float32
    )
    new_shard = (
        old_shard
        - learn_rate
        * (corrected_one / (jnp.sqrt(corrected_two) + epsilon) + decay_rate * old_shard)
    ).astype(jnp.bfloat16)

    partial_out = lax.dot_general(
        next_all, new_shard, (((1,), (1,)), ((), ())), preferred_element_type=jnp.float32
    )
    summed = lax.psum_scatter(partial_out, "tensor", scatter_dimension=0, tiled=True).astype(
        jnp.bfloat16
    )
    sub = me % group
    pieces = []
    for k in range(group):
        s = (sub + k) % group
        piece = lax.dynamic_slice_in_dim(summed, s * tok, tok, 0)
        perm = []
        for i in range(n_dp):
            for j in range(n_t):
                si = (i % group + k) % group
                dst = (group * j + si) * n_t + i // group
                perm.append((i * n_t + j, dst))
        pieces.append(lax.ppermute(piece, ("dp", "tensor"), perm))
    ordered = []
    for r in range(group):
        chosen = pieces[0]
        for k in range(1, group):
            chosen = jnp.where((sub - k) % group == r, pieces[k], chosen)
        ordered.append(chosen)
    next_out = jnp.concatenate(ordered, axis=1)
    return (gate_grad, up_grad, moment_one, moment_two, next_out)


def solution(mesh):
    n_dp = mesh.shape["dp"]
    n_t = mesh.shape["tensor"]
    if n_dp % n_t:
        raise ValueError("bad mesh")
    placed = (
        P("dp", None),
        P("dp", "tensor"),
        P("dp", "tensor"),
        P("dp", "tensor"),
        P(None, "tensor"),
        P("dp", "tensor"),
        P("dp", "tensor"),
    )
    return jax.shard_map(
        shards,
        mesh=mesh,
        in_specs=placed,
        out_specs=(
            P("dp", "tensor"),
            P("dp", "tensor"),
            P("dp", "tensor"),
            P("dp", "tensor"),
            P("dp", "tensor"),
        ),
        check_vma=False,
    )
```

```python
import jax
import jax.numpy as jnp
from jax import lax
from jax.sharding import PartitionSpec as P

STEP = 20


beta_one = 0.9
beta_two = 0.95
learn_rate = 0.001
decay_rate = 0.1
epsilon = 1e-08


def shards(grad_out, gate_input, up_input, next_hidden, down_weight, first_moment, second_moment):
    n_dp = lax.axis_size("dp")
    n_t = lax.axis_size("tensor")
    me = lax.axis_index("dp")
    col = lax.axis_index("tensor")
    tok = grad_out.shape[0]
    owned_rows = first_moment.shape[0]
    group = n_dp // n_t

    gate_value = gate_input.astype(jnp.float32)
    up_value = up_input.astype(jnp.float32)
    sigmoid_gate = jax.nn.sigmoid(gate_value)
    activated = gate_value * sigmoid_gate
    hidden = (activated * up_value).astype(jnp.bfloat16)

    hidden_all = lax.all_gather(hidden, "dp", axis=0, tiled=True)
    next_all = lax.all_gather(next_hidden, "dp", axis=0, tiled=True)
    grad_rows = lax.all_to_all(grad_out.T, "dp", 0, 1, tiled=True)

    grad_hidden = jnp.dot(grad_out, down_weight, preferred_element_type=jnp.float32)
    gate_grad = (
        grad_hidden * up_value * sigmoid_gate * (1.0 + gate_value * (1.0 - sigmoid_gate))
    ).astype(jnp.bfloat16)
    up_grad = (grad_hidden * activated).astype(jnp.bfloat16)

    weight_grad = jnp.zeros((owned_rows, hidden.shape[1]), jnp.float32)
    for b in range(n_dp):
        block = jnp.dot(
            grad_rows[:, b * tok : (b + 1) * tok],
            hidden_all[b * tok : (b + 1) * tok],
            preferred_element_type=jnp.float32,
        ).astype(jnp.bfloat16)
        weight_grad = weight_grad + block.astype(jnp.float32)

    moment_one = beta_one * first_moment + (1.0 - beta_one) * weight_grad
    moment_two = beta_two * second_moment + (1.0 - beta_two) * weight_grad * weight_grad
    corrected_one = moment_one / (1.0 - beta_one**STEP)
    corrected_two = moment_two / (1.0 - beta_two**STEP)
    old_shard = lax.dynamic_slice_in_dim(down_weight, me * owned_rows, owned_rows, 0).astype(
        jnp.float32
    )
    new_shard = (
        old_shard
        - learn_rate
        * (corrected_one / (jnp.sqrt(corrected_two) + epsilon) + decay_rate * old_shard)
    ).astype(jnp.bfloat16)

    partial_out = lax.dot_general(
        new_shard, next_all, (((1,), (1,)), ((), ())), preferred_element_type=jnp.float32
    )
    summed = (
        lax.psum_scatter(partial_out, "tensor", scatter_dimension=1, tiled=True)
        .astype(jnp.bfloat16)
        .T
    )
    sub = me % group
    pieces = []
    for k in range(group):
        s = (sub + k) % group
        piece = lax.dynamic_slice_in_dim(summed, s * tok, tok, 0)
        perm = []
        for i in range(n_dp):
            for j in range(n_t):
                si = (i % group + k) % group
                dst = (group * j + si) * n_t + i // group
                perm.append((i * n_t + j, dst))
        pieces.append(lax.ppermute(piece, ("dp", "tensor"), perm))
    ordered = []
    for r in range(group):
        chosen = pieces[0]
        for k in range(1, group):
            chosen = jnp.where((sub - k) % group == r, pieces[k], chosen)
        ordered.append(chosen)
    next_out = jnp.concatenate(ordered, axis=1)
    return (gate_grad, up_grad, moment_one, moment_two, next_out)


def solution(mesh):
    n_dp = mesh.shape["dp"]
    n_t = mesh.shape["tensor"]
    if n_dp % n_t:
        raise ValueError("bad mesh")
    placed = (
        P("dp", None),
        P("dp", "tensor"),
        P("dp", "tensor"),
        P("dp", "tensor"),
        P(None, "tensor"),
        P("dp", "tensor"),
        P("dp", "tensor"),
    )
    return jax.shard_map(
        shards,
        mesh=mesh,
        in_specs=placed,
        out_specs=(
            P("dp", "tensor"),
            P("dp", "tensor"),
            P("dp", "tensor"),
            P("dp", "tensor"),
            P("dp", "tensor"),
        ),
        check_vma=False,
    )
```

```python
import functools

import jax
import jax.numpy as jnp
from jax import lax
from jax.experimental import pallas as pl
from jax.experimental.pallas import tpu as pltpu
from jax.sharding import PartitionSpec as P

STEP = 20


beta_one = 0.9
beta_two = 0.95
learn_rate = 0.001
decay_rate = 0.1
epsilon = 1e-08


def adam_kernel(me_ref, g_ref, h_ref, m1_ref, m2_ref, w_ref, m1_out, m2_out, w_out, *, blocks, tok):
    acc = jnp.zeros(m1_ref.shape, jnp.float32)
    for b in range(blocks):
        part = jnp.dot(
            g_ref[:, b * tok : (b + 1) * tok],
            h_ref[b * tok : (b + 1) * tok, :],
            preferred_element_type=jnp.float32,
        )
        acc = acc + part.astype(jnp.bfloat16).astype(jnp.float32)
    moment_one = beta_one * m1_ref[...] + (1.0 - beta_one) * acc
    moment_two = beta_two * m2_ref[...] + (1.0 - beta_two) * acc * acc
    corrected_one = moment_one / (1.0 - beta_one**STEP)
    corrected_two = moment_two / (1.0 - beta_two**STEP)
    old = w_ref[...].astype(jnp.float32)
    w_out[...] = (
        old - learn_rate * (corrected_one / (jnp.sqrt(corrected_two) + epsilon) + decay_rate * old)
    ).astype(jnp.bfloat16)
    m1_out[...] = moment_one
    m2_out[...] = moment_two


def owner_update(me, grad_rows, hidden_all, first_moment, second_moment, down_weight, tok):
    rows, width = first_moment.shape
    tokens = hidden_all.shape[0]
    tn = 512 if width % 512 == 0 else 256
    grid_spec = pltpu.PrefetchScalarGridSpec(
        num_scalar_prefetch=1,
        grid=(width // tn,),
        in_specs=[
            pl.BlockSpec((rows, tokens), lambda n, me: (0, 0)),
            pl.BlockSpec((tokens, tn), lambda n, me: (0, n)),
            pl.BlockSpec((rows, tn), lambda n, me: (0, n)),
            pl.BlockSpec((rows, tn), lambda n, me: (0, n)),
            pl.BlockSpec((rows, tn), lambda n, me: (me[0], n)),
        ],
        out_specs=[
            pl.BlockSpec((rows, tn), lambda n, me: (0, n)),
            pl.BlockSpec((rows, tn), lambda n, me: (0, n)),
            pl.BlockSpec((rows, tn), lambda n, me: (0, n)),
        ],
    )
    flops = 2 * rows * tokens * width
    nbytes = 2 * rows * tokens + 2 * tokens * width + 16 * rows * width + 4 * rows * width
    return pl.pallas_call(
        functools.partial(adam_kernel, blocks=tokens // tok, tok=tok),
        grid_spec=grid_spec,
        out_shape=[
            jax.ShapeDtypeStruct((rows, width), jnp.float32),
            jax.ShapeDtypeStruct((rows, width), jnp.float32),
            jax.ShapeDtypeStruct((rows, width), jnp.bfloat16),
        ],
        compiler_params=pltpu.CompilerParams(vmem_limit_bytes=48 * 1024 * 1024),
        cost_estimate=pl.CostEstimate(flops=flops, transcendentals=rows * width, bytes_accessed=nbytes),
    )(jnp.reshape(me, (1,)).astype(jnp.int32), grad_rows, hidden_all, first_moment, second_moment, down_weight)


def shards(grad_out, gate_input, up_input, next_hidden, down_weight, first_moment, second_moment):
    n_dp = lax.axis_size("dp")
    n_t = lax.axis_size("tensor")
    me = lax.axis_index("dp")
    col = lax.axis_index("tensor")
    tok = grad_out.shape[0]
    owned_rows = first_moment.shape[0]
    group = n_dp // n_t

    gate_value = gate_input.astype(jnp.float32)
    up_value = up_input.astype(jnp.float32)
    sigmoid_gate = jax.nn.sigmoid(gate_value)
    activated = gate_value * sigmoid_gate
    hidden = (activated * up_value).astype(jnp.bfloat16)
    hidden, gate_input, up_input = lax.optimization_barrier((hidden, gate_input, up_input))
    gate_value = gate_input.astype(jnp.float32)
    up_value = up_input.astype(jnp.float32)
    sigmoid_gate = jax.nn.sigmoid(gate_value)
    activated = gate_value * sigmoid_gate

    hidden_all = lax.all_gather(hidden, "dp", axis=0, tiled=True)
    next_all = lax.all_gather(next_hidden, "dp", axis=0, tiled=True)
    grad_rows = lax.all_to_all(grad_out.T, "dp", 0, 1, tiled=True)

    grad_hidden = jnp.dot(grad_out, down_weight, preferred_element_type=jnp.float32)
    gate_grad = (
        grad_hidden * up_value * sigmoid_gate * (1.0 + gate_value * (1.0 - sigmoid_gate))
    ).astype(jnp.bfloat16)
    up_grad = (grad_hidden * activated).astype(jnp.bfloat16)

    moment_one, moment_two, new_shard = owner_update(
        me, grad_rows, hidden_all, first_moment, second_moment, down_weight, tok
    )

    partial_out = lax.dot_general(
        new_shard, next_all, (((1,), (1,)), ((), ())), preferred_element_type=jnp.float32
    )
    summed = (
        lax.psum_scatter(partial_out, "tensor", scatter_dimension=1, tiled=True)
        .astype(jnp.bfloat16)
        .T
    )
    sub = me % group
    pieces = []
    for k in range(group):
        s = (sub + k) % group
        piece = lax.dynamic_slice_in_dim(summed, s * tok, tok, 0)
        perm = []
        for i in range(n_dp):
            for j in range(n_t):
                si = (i % group + k) % group
                dst = (group * j + si) * n_t + i // group
                perm.append((i * n_t + j, dst))
        pieces.append(lax.ppermute(piece, ("dp", "tensor"), perm))
    ordered = []
    for r in range(group):
        chosen = pieces[0]
        for k in range(1, group):
            chosen = jnp.where((sub - k) % group == r, pieces[k], chosen)
        ordered.append(chosen)
    next_out = jnp.concatenate(ordered, axis=1)
    return (gate_grad, up_grad, moment_one, moment_two, next_out)


def solution(mesh):
    n_dp = mesh.shape["dp"]
    n_t = mesh.shape["tensor"]
    if n_dp % n_t:
        raise ValueError("bad mesh")
    placed = (
        P("dp", None),
        P("dp", "tensor"),
        P("dp", "tensor"),
        P("dp", "tensor"),
        P(None, "tensor"),
        P("dp", "tensor"),
        P("dp", "tensor"),
    )
    return jax.shard_map(
        shards,
        mesh=mesh,
        in_specs=placed,
        out_specs=(
            P("dp", "tensor"),
            P("dp", "tensor"),
            P("dp", "tensor"),
            P("dp", "tensor"),
            P("dp", "tensor"),
        ),
        check_vma=False,
    )
```

```python
import functools

import jax
import jax.numpy as jnp
from jax import lax
from jax.experimental import pallas as pl
from jax.experimental.pallas import tpu as pltpu
from jax.sharding import PartitionSpec as P

STEP = 20


beta_one = 0.9
beta_two = 0.95
learn_rate = 0.001
decay_rate = 0.1
epsilon = 1e-08


def adam_kernel(me_ref, g_ref, h_ref, m1_ref, m2_ref, w_ref, m1_out, m2_out, w_out, *, blocks, tok):
    acc = jnp.zeros(m1_ref.shape, jnp.float32)
    for b in range(blocks):
        part = jnp.dot(
            g_ref[:, b * tok : (b + 1) * tok],
            h_ref[b * tok : (b + 1) * tok, :],
            preferred_element_type=jnp.float32,
        )
        acc = acc + part.astype(jnp.bfloat16).astype(jnp.float32)
    moment_one = beta_one * m1_ref[...] + (1.0 - beta_one) * acc
    moment_two = beta_two * m2_ref[...] + (1.0 - beta_two) * acc * acc
    corrected_one = moment_one / (1.0 - beta_one**STEP)
    corrected_two = moment_two / (1.0 - beta_two**STEP)
    old = w_ref[...].astype(jnp.float32)
    w_out[...] = (
        old - learn_rate * (corrected_one / (jnp.sqrt(corrected_two) + epsilon) + decay_rate * old)
    ).astype(jnp.bfloat16)
    m1_out[...] = moment_one
    m2_out[...] = moment_two


def owner_update(me, grad_rows, hidden_all, first_moment, second_moment, down_weight, tok):
    rows, width = first_moment.shape
    tokens = hidden_all.shape[0]
    tn = 512 if width % 512 == 0 else 256
    grid_spec = pltpu.PrefetchScalarGridSpec(
        num_scalar_prefetch=1,
        grid=(width // tn,),
        in_specs=[
            pl.BlockSpec((rows, tokens), lambda n, me: (0, 0)),
            pl.BlockSpec((tokens, tn), lambda n, me: (0, n)),
            pl.BlockSpec((rows, tn), lambda n, me: (0, n)),
            pl.BlockSpec((rows, tn), lambda n, me: (0, n)),
            pl.BlockSpec((rows, tn), lambda n, me: (me[0], n)),
        ],
        out_specs=[
            pl.BlockSpec((rows, tn), lambda n, me: (0, n)),
            pl.BlockSpec((rows, tn), lambda n, me: (0, n)),
            pl.BlockSpec((rows, tn), lambda n, me: (0, n)),
        ],
    )
    flops = 2 * rows * tokens * width
    nbytes = 2 * rows * tokens + 2 * tokens * width + 16 * rows * width + 4 * rows * width
    return pl.pallas_call(
        functools.partial(adam_kernel, blocks=tokens // tok, tok=tok),
        grid_spec=grid_spec,
        out_shape=[
            jax.ShapeDtypeStruct((rows, width), jnp.float32),
            jax.ShapeDtypeStruct((rows, width), jnp.float32),
            jax.ShapeDtypeStruct((rows, width), jnp.bfloat16),
        ],
        compiler_params=pltpu.CompilerParams(vmem_limit_bytes=48 * 1024 * 1024),
        cost_estimate=pl.CostEstimate(flops=flops, transcendentals=rows * width, bytes_accessed=nbytes),
    )(jnp.reshape(me, (1,)).astype(jnp.int32), grad_rows, hidden_all, first_moment, second_moment, down_weight)


def shards(grad_out, gate_input, up_input, next_hidden, down_weight, first_moment, second_moment):
    n_dp = lax.axis_size("dp")
    n_t = lax.axis_size("tensor")
    me = lax.axis_index("dp")
    col = lax.axis_index("tensor")
    tok = grad_out.shape[0]
    owned_rows = first_moment.shape[0]
    group = n_dp // n_t

    gate_value = gate_input.astype(jnp.float32)
    up_value = up_input.astype(jnp.float32)
    sigmoid_gate = jax.nn.sigmoid(gate_value)
    activated = gate_value * sigmoid_gate
    hidden = (activated * up_value).astype(jnp.bfloat16)
    hidden, gate_input, up_input = lax.optimization_barrier((hidden, gate_input, up_input))
    gate_value = gate_input.astype(jnp.float32)
    up_value = up_input.astype(jnp.float32)
    sigmoid_gate = jax.nn.sigmoid(gate_value)
    activated = gate_value * sigmoid_gate

    half = tok // 2
    hidden_all = lax.all_gather(hidden, "dp", axis=0, tiled=True)
    first_own, hidden_all = lax.optimization_barrier((next_hidden[:half], hidden_all))
    first_next = lax.all_gather(first_own, "dp", axis=0, tiled=True)
    grad_rows = lax.all_to_all(grad_out.T, "dp", 0, 1, tiled=True)

    grad_hidden = jnp.dot(grad_out, down_weight, preferred_element_type=jnp.float32)
    gate_grad = (
        grad_hidden * up_value * sigmoid_gate * (1.0 + gate_value * (1.0 - sigmoid_gate))
    ).astype(jnp.bfloat16)
    up_grad = (grad_hidden * activated).astype(jnp.bfloat16)

    moment_one, moment_two, new_shard = owner_update(
        me, grad_rows, hidden_all, first_moment, second_moment, down_weight, tok
    )
    gate_grad, up_grad, new_shard = lax.optimization_barrier((gate_grad, up_grad, new_shard))

    width = n_dp * half // n_t
    summed_parts = []
    next_part = first_next
    for c in range(2):
        partial_out = lax.dot_general(
            new_shard, next_part, (((1,), (1,)), ((), ())), preferred_element_type=jnp.float32
        )
        if c == 0:
            second_own, partial_out = lax.optimization_barrier((next_hidden[half:], partial_out))
            next_part = lax.all_gather(second_own, "dp", axis=0, tiled=True)
            blocks = lax.all_to_all(partial_out, "tensor", 1, 0, tiled=True)
            blocks, next_part = lax.optimization_barrier((blocks, next_part))
            total = jnp.sum(jnp.reshape(blocks, (n_t,) + partial_out.shape[:1] + (width,)), axis=0)
        else:
            total = lax.psum_scatter(partial_out, "tensor", scatter_dimension=1, tiled=True)
        summed_parts.append(total.astype(jnp.bfloat16).T)

    sub = me % group
    halves = []
    for c in range(2):
        pieces = []
        for k in range(group):
            s = (sub + k) % group
            piece = lax.dynamic_slice_in_dim(summed_parts[c], s * half, half, 0)
            perm = []
            for i in range(n_dp):
                for j in range(n_t):
                    si = (i % group + k) % group
                    dst = (group * j + si) * n_t + i // group
                    perm.append((i * n_t + j, dst))
            pieces.append(lax.ppermute(piece, ("dp", "tensor"), perm))
        ordered = []
        for r in range(group):
            chosen = pieces[0]
            for k in range(1, group):
                chosen = jnp.where((sub - k) % group == r, pieces[k], chosen)
            ordered.append(chosen)
        halves.append(jnp.concatenate(ordered, axis=1))
    next_out = jnp.concatenate(halves, axis=0)
    return (gate_grad, up_grad, moment_one, moment_two, next_out)


def solution(mesh):
    n_dp = mesh.shape["dp"]
    n_t = mesh.shape["tensor"]
    if n_dp % n_t:
        raise ValueError("bad mesh")
    placed = (
        P("dp", None),
        P("dp", "tensor"),
        P("dp", "tensor"),
        P("dp", "tensor"),
        P(None, "tensor"),
        P("dp", "tensor"),
        P("dp", "tensor"),
    )
    return jax.shard_map(
        shards,
        mesh=mesh,
        in_specs=placed,
        out_specs=(
            P("dp", "tensor"),
            P("dp", "tensor"),
            P("dp", "tensor"),
            P("dp", "tensor"),
            P("dp", "tensor"),
        ),
        check_vma=False,
    )
```

```python
import functools

import jax
import jax.numpy as jnp
from jax import lax
from jax.experimental import pallas as pl
from jax.experimental.pallas import tpu as pltpu
from jax.sharding import PartitionSpec as P

STEP = 20


beta_one = 0.9
beta_two = 0.95
learn_rate = 0.001
decay_rate = 0.1
epsilon = 1e-08


def adam_kernel(me_ref, g_ref, h_ref, m1_ref, m2_ref, w_ref, m1_out, m2_out, w_out, *, blocks, tok):
    acc = jnp.zeros(m1_ref.shape, jnp.float32)
    for b in range(blocks):
        part = jnp.dot(
            g_ref[:, b * tok : (b + 1) * tok],
            h_ref[b * tok : (b + 1) * tok, :],
            preferred_element_type=jnp.float32,
        )
        acc = acc + part.astype(jnp.bfloat16).astype(jnp.float32)
    moment_one = beta_one * m1_ref[...] + (1.0 - beta_one) * acc
    moment_two = beta_two * m2_ref[...] + (1.0 - beta_two) * acc * acc
    corrected_one = moment_one / (1.0 - beta_one**STEP)
    corrected_two = moment_two / (1.0 - beta_two**STEP)
    old = w_ref[...].astype(jnp.float32)
    w_out[...] = (
        old - learn_rate * (corrected_one / (jnp.sqrt(corrected_two) + epsilon) + decay_rate * old)
    ).astype(jnp.bfloat16)
    m1_out[...] = moment_one
    m2_out[...] = moment_two


def owner_update(me, grad_rows, hidden_all, first_moment, second_moment, down_weight, tok):
    rows, width = first_moment.shape
    tokens = hidden_all.shape[0]
    tn = 512 if width % 512 == 0 else 256
    grid_spec = pltpu.PrefetchScalarGridSpec(
        num_scalar_prefetch=1,
        grid=(width // tn,),
        in_specs=[
            pl.BlockSpec((rows, tokens), lambda n, me: (0, 0)),
            pl.BlockSpec((tokens, tn), lambda n, me: (0, n)),
            pl.BlockSpec((rows, tn), lambda n, me: (0, n)),
            pl.BlockSpec((rows, tn), lambda n, me: (0, n)),
            pl.BlockSpec((rows, tn), lambda n, me: (me[0], n)),
        ],
        out_specs=[
            pl.BlockSpec((rows, tn), lambda n, me: (0, n)),
            pl.BlockSpec((rows, tn), lambda n, me: (0, n)),
            pl.BlockSpec((rows, tn), lambda n, me: (0, n)),
        ],
    )
    flops = 2 * rows * tokens * width
    nbytes = 2 * rows * tokens + 2 * tokens * width + 16 * rows * width + 4 * rows * width
    return pl.pallas_call(
        functools.partial(adam_kernel, blocks=tokens // tok, tok=tok),
        grid_spec=grid_spec,
        out_shape=[
            jax.ShapeDtypeStruct((rows, width), jnp.float32),
            jax.ShapeDtypeStruct((rows, width), jnp.float32),
            jax.ShapeDtypeStruct((rows, width), jnp.bfloat16),
        ],
        compiler_params=pltpu.CompilerParams(vmem_limit_bytes=48 * 1024 * 1024),
        cost_estimate=pl.CostEstimate(flops=flops, transcendentals=rows * width, bytes_accessed=nbytes),
    )(jnp.reshape(me, (1,)).astype(jnp.int32), grad_rows, hidden_all, first_moment, second_moment, down_weight)


def shards(grad_out, gate_input, up_input, next_hidden, down_weight, first_moment, second_moment):
    n_dp = lax.axis_size("dp")
    n_t = lax.axis_size("tensor")
    me = lax.axis_index("dp")
    col = lax.axis_index("tensor")
    tok = grad_out.shape[0]
    owned_rows = first_moment.shape[0]
    group = n_dp // n_t

    gate_value = gate_input.astype(jnp.float32)
    up_value = up_input.astype(jnp.float32)
    sigmoid_gate = jax.nn.sigmoid(gate_value)
    activated = gate_value * sigmoid_gate
    hidden = (activated * up_value).astype(jnp.bfloat16)
    hidden, gate_input, up_input = lax.optimization_barrier((hidden, gate_input, up_input))
    gate_value = gate_input.astype(jnp.float32)
    up_value = up_input.astype(jnp.float32)
    sigmoid_gate = jax.nn.sigmoid(gate_value)
    activated = gate_value * sigmoid_gate

    half = tok // 2
    hidden_all = lax.all_gather(hidden, "dp", axis=0, tiled=True)
    first_own, hidden_all = lax.optimization_barrier((next_hidden[:half], hidden_all))
    first_next = lax.all_gather(first_own, "dp", axis=0, tiled=True)
    second_own, first_next = lax.optimization_barrier((next_hidden[half:], first_next))
    next_part = lax.all_gather(second_own, "dp", axis=0, tiled=True)
    grad_rows = lax.all_to_all(grad_out.T, "dp", 0, 1, tiled=True)

    grad_hidden = jnp.dot(grad_out, down_weight, preferred_element_type=jnp.float32)
    gate_grad = (
        grad_hidden * up_value * sigmoid_gate * (1.0 + gate_value * (1.0 - sigmoid_gate))
    ).astype(jnp.bfloat16)
    up_grad = (grad_hidden * activated).astype(jnp.bfloat16)

    moment_one, moment_two, new_shard = owner_update(
        me, grad_rows, hidden_all, first_moment, second_moment, down_weight, tok
    )
    gate_grad, up_grad, new_shard = lax.optimization_barrier((gate_grad, up_grad, new_shard))

    width = n_dp * half // n_t
    summed_parts = []
    for c in range(2):
        partial_out = lax.dot_general(
            new_shard, first_next if c == 0 else next_part, (((1,), (1,)), ((), ())), preferred_element_type=jnp.float32
        )
        if c == 0:
            blocks = lax.all_to_all(partial_out, "tensor", 1, 0, tiled=True)
            blocks, next_part = lax.optimization_barrier((blocks, next_part))
            blocks = jnp.reshape(blocks, (n_t,) + partial_out.shape[:1] + (width,))
            total = jnp.sum(blocks, axis=0)
        else:
            total = lax.dynamic_slice_in_dim(partial_out, col * width, width, 1)
            for s in range(1, n_t):
                block = lax.dynamic_slice_in_dim(partial_out, ((col + s) % n_t) * width, width, 1)
                moved = lax.ppermute(block, "tensor", [(j, (j + s) % n_t) for j in range(n_t)])
                total = total + moved
        summed_parts.append(total.astype(jnp.bfloat16).T)

    sub = me % group
    halves = []
    for c in range(2):
        pieces = []
        for k in range(group):
            s = (sub + k) % group
            piece = lax.dynamic_slice_in_dim(summed_parts[c], s * half, half, 0)
            perm = []
            for i in range(n_dp):
                for j in range(n_t):
                    si = (i % group + k) % group
                    dst = (group * j + si) * n_t + i // group
                    perm.append((i * n_t + j, dst))
            pieces.append(lax.ppermute(piece, ("dp", "tensor"), perm))
        ordered = []
        for r in range(group):
            chosen = pieces[0]
            for k in range(1, group):
                chosen = jnp.where((sub - k) % group == r, pieces[k], chosen)
            ordered.append(chosen)
        halves.append(jnp.concatenate(ordered, axis=1))
    next_out = jnp.concatenate(halves, axis=0)
    return (gate_grad, up_grad, moment_one, moment_two, next_out)


def solution(mesh):
    n_dp = mesh.shape["dp"]
    n_t = mesh.shape["tensor"]
    if n_dp % n_t:
        raise ValueError("bad mesh")
    placed = (
        P("dp", None),
        P("dp", "tensor"),
        P("dp", "tensor"),
        P("dp", "tensor"),
        P(None, "tensor"),
        P("dp", "tensor"),
        P("dp", "tensor"),
    )
    return jax.shard_map(
        shards,
        mesh=mesh,
        in_specs=placed,
        out_specs=(
            P("dp", "tensor"),
            P("dp", "tensor"),
            P("dp", "tensor"),
            P("dp", "tensor"),
            P("dp", "tensor"),
        ),
        check_vma=False,
    )
```

```python
import functools

import jax
import jax.numpy as jnp
from jax import lax
from jax.experimental import pallas as pl
from jax.experimental.pallas import tpu as pltpu
from jax.sharding import PartitionSpec as P

STEP = 20


beta_one = 0.9
beta_two = 0.95
learn_rate = 0.001
decay_rate = 0.1
epsilon = 1e-08


def adam_kernel(me_ref, g_ref, h_ref, m1_ref, m2_ref, w_ref, m1_out, m2_out, w_out, *, blocks, tok):
    acc = jnp.zeros(m1_ref.shape, jnp.float32)
    for b in range(blocks):
        part = jnp.dot(
            g_ref[:, b * tok : (b + 1) * tok],
            h_ref[b * tok : (b + 1) * tok, :],
            preferred_element_type=jnp.float32,
        )
        acc = acc + part.astype(jnp.bfloat16).astype(jnp.float32)
    moment_one = beta_one * m1_ref[...] + (1.0 - beta_one) * acc
    moment_two = beta_two * m2_ref[...] + (1.0 - beta_two) * acc * acc
    corrected_one = moment_one / (1.0 - beta_one**STEP)
    corrected_two = moment_two / (1.0 - beta_two**STEP)
    old = w_ref[...].astype(jnp.float32)
    w_out[...] = (
        old - learn_rate * (corrected_one / (jnp.sqrt(corrected_two) + epsilon) + decay_rate * old)
    ).astype(jnp.bfloat16)
    m1_out[...] = moment_one
    m2_out[...] = moment_two


def owner_update(me, grad_rows, hidden_all, first_moment, second_moment, down_weight, tok):
    rows, width = first_moment.shape
    tokens = hidden_all.shape[0]
    tn = 512 if width % 512 == 0 else 256
    grid_spec = pltpu.PrefetchScalarGridSpec(
        num_scalar_prefetch=1,
        grid=(width // tn,),
        in_specs=[
            pl.BlockSpec((rows, tokens), lambda n, me: (0, 0)),
            pl.BlockSpec((tokens, tn), lambda n, me: (0, n)),
            pl.BlockSpec((rows, tn), lambda n, me: (0, n)),
            pl.BlockSpec((rows, tn), lambda n, me: (0, n)),
            pl.BlockSpec((rows, tn), lambda n, me: (me[0], n)),
        ],
        out_specs=[
            pl.BlockSpec((rows, tn), lambda n, me: (0, n)),
            pl.BlockSpec((rows, tn), lambda n, me: (0, n)),
            pl.BlockSpec((rows, tn), lambda n, me: (0, n)),
        ],
    )
    flops = 2 * rows * tokens * width
    nbytes = 2 * rows * tokens + 2 * tokens * width + 16 * rows * width + 4 * rows * width
    return pl.pallas_call(
        functools.partial(adam_kernel, blocks=tokens // tok, tok=tok),
        grid_spec=grid_spec,
        out_shape=[
            jax.ShapeDtypeStruct((rows, width), jnp.float32),
            jax.ShapeDtypeStruct((rows, width), jnp.float32),
            jax.ShapeDtypeStruct((rows, width), jnp.bfloat16),
        ],
        compiler_params=pltpu.CompilerParams(vmem_limit_bytes=48 * 1024 * 1024),
        cost_estimate=pl.CostEstimate(flops=flops, transcendentals=rows * width, bytes_accessed=nbytes),
    )(jnp.reshape(me, (1,)).astype(jnp.int32), grad_rows, hidden_all, first_moment, second_moment, down_weight)


def shards(grad_out, gate_input, up_input, next_hidden, down_weight, first_moment, second_moment):
    n_dp = lax.axis_size("dp")
    n_t = lax.axis_size("tensor")
    me = lax.axis_index("dp")
    col = lax.axis_index("tensor")
    tok = grad_out.shape[0]
    owned_rows = first_moment.shape[0]
    group = n_dp // n_t

    gate_value = gate_input.astype(jnp.float32)
    up_value = up_input.astype(jnp.float32)
    sigmoid_gate = jax.nn.sigmoid(gate_value)
    activated = gate_value * sigmoid_gate
    hidden = (activated * up_value).astype(jnp.bfloat16)
    hidden, gate_input, up_input = lax.optimization_barrier((hidden, gate_input, up_input))
    gate_value = gate_input.astype(jnp.float32)
    up_value = up_input.astype(jnp.float32)
    sigmoid_gate = jax.nn.sigmoid(gate_value)
    activated = gate_value * sigmoid_gate

    half = tok // 2
    hidden_all = lax.all_gather(hidden, "dp", axis=0, tiled=True)
    first_own, hidden_all = lax.optimization_barrier((next_hidden[:half], hidden_all))
    first_next = lax.all_gather(first_own, "dp", axis=0, tiled=True)
    grad_rows = lax.all_to_all(grad_out.T, "dp", 0, 1, tiled=True)

    grad_hidden = jnp.dot(grad_out, down_weight, preferred_element_type=jnp.float32)
    gate_grad = (
        grad_hidden * up_value * sigmoid_gate * (1.0 + gate_value * (1.0 - sigmoid_gate))
    ).astype(jnp.bfloat16)
    up_grad = (grad_hidden * activated).astype(jnp.bfloat16)

    moment_one, moment_two, new_shard = owner_update(
        me, grad_rows, hidden_all, first_moment, second_moment, down_weight, tok
    )
    gate_grad, up_grad, new_shard = lax.optimization_barrier((gate_grad, up_grad, new_shard))

    width = n_dp * half // n_t
    summed_parts = []
    next_part = first_next
    for c in range(2):
        partial_out = lax.dot_general(
            new_shard, next_part, (((1,), (1,)), ((), ())), preferred_element_type=jnp.float32
        )
        if c == 0:
            second_own, partial_out = lax.optimization_barrier((next_hidden[half:], partial_out))
            next_part = lax.all_gather(second_own, "dp", axis=0, tiled=True)
            blocks = lax.all_to_all(partial_out, "tensor", 1, 0, tiled=True)
            blocks, next_part = lax.optimization_barrier((blocks, next_part))
            total = jnp.sum(jnp.reshape(blocks, (n_t,) + partial_out.shape[:1] + (width,)), axis=0)
        else:
            total = lax.dynamic_slice_in_dim(partial_out, col * width, width, 1)
            for s in range(1, n_t):
                block = lax.dynamic_slice_in_dim(partial_out, ((col + s) % n_t) * width, width, 1)
                total = total + lax.ppermute(
                    block, "tensor", [(j, (j + s) % n_t) for j in range(n_t)]
                )
        summed_parts.append(total.astype(jnp.bfloat16).T)

    sub = me % group
    halves = []
    for c in range(2):
        pieces = []
        for k in range(group):
            s = (sub + k) % group
            piece = lax.dynamic_slice_in_dim(summed_parts[c], s * half, half, 0)
            perm = []
            for i in range(n_dp):
                for j in range(n_t):
                    si = (i % group + k) % group
                    dst = (group * j + si) * n_t + i // group
                    perm.append((i * n_t + j, dst))
            pieces.append(lax.ppermute(piece, ("dp", "tensor"), perm))
        ordered = []
        for r in range(group):
            chosen = pieces[0]
            for k in range(1, group):
                chosen = jnp.where((sub - k) % group == r, pieces[k], chosen)
            ordered.append(chosen)
        halves.append(jnp.concatenate(ordered, axis=1))
    next_out = jnp.concatenate(halves, axis=0)
    return (gate_grad, up_grad, moment_one, moment_two, next_out)


def solution(mesh):
    n_dp = mesh.shape["dp"]
    n_t = mesh.shape["tensor"]
    if n_dp % n_t:
        raise ValueError("bad mesh")
    placed = (
        P("dp", None),
        P("dp", "tensor"),
        P("dp", "tensor"),
        P("dp", "tensor"),
        P(None, "tensor"),
        P("dp", "tensor"),
        P("dp", "tensor"),
    )
    return jax.shard_map(
        shards,
        mesh=mesh,
        in_specs=placed,
        out_specs=(
            P("dp", "tensor"),
            P("dp", "tensor"),
            P("dp", "tensor"),
            P("dp", "tensor"),
            P("dp", "tensor"),
        ),
        check_vma=False,
    )
```

```python
import functools

import jax
import jax.numpy as jnp
from jax import lax
from jax.experimental import pallas as pl
from jax.experimental.pallas import tpu as pltpu
from jax.sharding import PartitionSpec as P

STEP = 20


beta_one = 0.9
beta_two = 0.95
learn_rate = 0.001
decay_rate = 0.1
epsilon = 1e-08


def adam_kernel(me_ref, g_ref, h_ref, m1_ref, m2_ref, w_ref, m1_out, m2_out, w_out, *, blocks, tok):
    acc = jnp.zeros(m1_ref.shape, jnp.float32)
    for b in range(blocks):
        part = jnp.dot(
            g_ref[:, b * tok : (b + 1) * tok],
            h_ref[b * tok : (b + 1) * tok, :],
            preferred_element_type=jnp.float32,
        )
        acc = acc + part.astype(jnp.bfloat16).astype(jnp.float32)
    moment_one = beta_one * m1_ref[...] + (1.0 - beta_one) * acc
    moment_two = beta_two * m2_ref[...] + (1.0 - beta_two) * acc * acc
    corrected_one = moment_one / (1.0 - beta_one**STEP)
    corrected_two = moment_two / (1.0 - beta_two**STEP)
    old = w_ref[...].astype(jnp.float32)
    w_out[...] = (
        old - learn_rate * (corrected_one / (jnp.sqrt(corrected_two) + epsilon) + decay_rate * old)
    ).astype(jnp.bfloat16)
    m1_out[...] = moment_one
    m2_out[...] = moment_two


def owner_update(me, grad_rows, hidden_all, first_moment, second_moment, down_weight, tok):
    rows, width = first_moment.shape
    tokens = hidden_all.shape[0]
    tn = 512 if width % 512 == 0 else 256
    grid_spec = pltpu.PrefetchScalarGridSpec(
        num_scalar_prefetch=1,
        grid=(width // tn,),
        in_specs=[
            pl.BlockSpec((rows, tokens), lambda n, me: (0, 0)),
            pl.BlockSpec((tokens, tn), lambda n, me: (0, n)),
            pl.BlockSpec((rows, tn), lambda n, me: (0, n)),
            pl.BlockSpec((rows, tn), lambda n, me: (0, n)),
            pl.BlockSpec((rows, tn), lambda n, me: (me[0], n)),
        ],
        out_specs=[
            pl.BlockSpec((rows, tn), lambda n, me: (0, n)),
            pl.BlockSpec((rows, tn), lambda n, me: (0, n)),
            pl.BlockSpec((rows, tn), lambda n, me: (0, n)),
        ],
    )
    flops = 2 * rows * tokens * width
    nbytes = 2 * rows * tokens + 2 * tokens * width + 16 * rows * width + 4 * rows * width
    return pl.pallas_call(
        functools.partial(adam_kernel, blocks=tokens // tok, tok=tok),
        grid_spec=grid_spec,
        out_shape=[
            jax.ShapeDtypeStruct((rows, width), jnp.float32),
            jax.ShapeDtypeStruct((rows, width), jnp.float32),
            jax.ShapeDtypeStruct((rows, width), jnp.bfloat16),
        ],
        compiler_params=pltpu.CompilerParams(vmem_limit_bytes=48 * 1024 * 1024),
        cost_estimate=pl.CostEstimate(flops=flops, transcendentals=rows * width, bytes_accessed=nbytes),
    )(jnp.reshape(me, (1,)).astype(jnp.int32), grad_rows, hidden_all, first_moment, second_moment, down_weight)


def gather_plane(x):
    half = x.shape[0] // 2

    def swap(v, k):
        return lax.ppermute(v, "dp", [(i, i ^ k) for i in range(8)])

    along_x = swap(x, 2)
    along_y = swap(x, 4)
    partner = swap(x, 1)
    diagonal = jnp.concatenate([swap(along_x[:half], 4), swap(along_y[half:], 2)], axis=0)
    blocks = [
        x,
        partner,
        along_x,
        swap(along_x, 1),
        along_y,
        swap(along_y, 1),
        diagonal,
        swap(diagonal, 1),
    ]
    return jnp.concatenate(blocks, axis=0)


def shards(grad_out, gate_input, up_input, next_hidden, down_weight, first_moment, second_moment):
    n_dp = lax.axis_size("dp")
    n_t = lax.axis_size("tensor")
    me = lax.axis_index("dp")
    col = lax.axis_index("tensor")
    tok = grad_out.shape[0]
    owned_rows = first_moment.shape[0]
    group = n_dp // n_t

    gate_value = gate_input.astype(jnp.float32)
    up_value = up_input.astype(jnp.float32)
    sigmoid_gate = jax.nn.sigmoid(gate_value)
    activated = gate_value * sigmoid_gate
    hidden = (activated * up_value).astype(jnp.bfloat16)
    hidden, gate_input, up_input = lax.optimization_barrier((hidden, gate_input, up_input))
    gate_value = gate_input.astype(jnp.float32)
    up_value = up_input.astype(jnp.float32)
    sigmoid_gate = jax.nn.sigmoid(gate_value)
    activated = gate_value * sigmoid_gate

    half = tok // 2
    plane = n_dp == 8
    if plane:
        hidden_all = gather_plane(hidden)
    else:
        hidden_all = lax.all_gather(hidden, "dp", axis=0, tiled=True)
    first_own, hidden_all = lax.optimization_barrier((next_hidden[:half], hidden_all))
    first_next = lax.all_gather(first_own, "dp", axis=0, tiled=True)
    grad_rows = lax.all_to_all(grad_out.T, "dp", 0, 1, tiled=True)
    if plane:
        grad_rows = jnp.concatenate(
            [lax.dynamic_slice_in_dim(grad_rows, (me ^ p) * tok, tok, 1) for p in range(n_dp)],
            axis=1,
        )

    grad_hidden = jnp.dot(grad_out, down_weight, preferred_element_type=jnp.float32)
    gate_grad = (
        grad_hidden * up_value * sigmoid_gate * (1.0 + gate_value * (1.0 - sigmoid_gate))
    ).astype(jnp.bfloat16)
    up_grad = (grad_hidden * activated).astype(jnp.bfloat16)

    moment_one, moment_two, new_shard = owner_update(
        me, grad_rows, hidden_all, first_moment, second_moment, down_weight, tok
    )
    gate_grad, up_grad, new_shard = lax.optimization_barrier((gate_grad, up_grad, new_shard))

    width = n_dp * half // n_t
    summed_parts = []
    next_part = first_next
    for c in range(2):
        partial_out = lax.dot_general(
            new_shard, next_part, (((1,), (1,)), ((), ())), preferred_element_type=jnp.float32
        )
        if c == 0:
            second_own, partial_out = lax.optimization_barrier((next_hidden[half:], partial_out))
            next_part = lax.all_gather(second_own, "dp", axis=0, tiled=True)
            blocks = lax.all_to_all(partial_out, "tensor", 1, 0, tiled=True)
            blocks, next_part = lax.optimization_barrier((blocks, next_part))
            total = jnp.sum(jnp.reshape(blocks, (n_t,) + partial_out.shape[:1] + (width,)), axis=0)
        else:
            total = lax.psum_scatter(partial_out, "tensor", scatter_dimension=1, tiled=True)
        summed_parts.append(total.astype(jnp.bfloat16).T)

    sub = me % group
    halves = []
    for c in range(2):
        pieces = []
        for k in range(group):
            s = (sub + k) % group
            piece = lax.dynamic_slice_in_dim(summed_parts[c], s * half, half, 0)
            perm = []
            for i in range(n_dp):
                for j in range(n_t):
                    si = (i % group + k) % group
                    dst = (group * j + si) * n_t + i // group
                    perm.append((i * n_t + j, dst))
            pieces.append(lax.ppermute(piece, ("dp", "tensor"), perm))
        ordered = []
        for r in range(group):
            chosen = pieces[0]
            for k in range(1, group):
                chosen = jnp.where((sub - k) % group == r, pieces[k], chosen)
            ordered.append(chosen)
        halves.append(jnp.concatenate(ordered, axis=1))
    next_out = jnp.concatenate(halves, axis=0)
    return (gate_grad, up_grad, moment_one, moment_two, next_out)


def solution(mesh):
    n_dp = mesh.shape["dp"]
    n_t = mesh.shape["tensor"]
    if n_dp % n_t:
        raise ValueError("bad mesh")
    placed = (
        P("dp", None),
        P("dp", "tensor"),
        P("dp", "tensor"),
        P("dp", "tensor"),
        P(None, "tensor"),
        P("dp", "tensor"),
        P("dp", "tensor"),
    )
    return jax.shard_map(
        shards,
        mesh=mesh,
        in_specs=placed,
        out_specs=(
            P("dp", "tensor"),
            P("dp", "tensor"),
            P("dp", "tensor"),
            P("dp", "tensor"),
            P("dp", "tensor"),
        ),
        check_vma=False,
    )
```

```python
import functools

import jax
import jax.numpy as jnp
from jax import lax
from jax.experimental import pallas as pl
from jax.experimental.pallas import tpu as pltpu
from jax.sharding import PartitionSpec as P

STEP = 20


beta_one = 0.9
beta_two = 0.95
learn_rate = 0.001
decay_rate = 0.1
epsilon = 1e-08


def adam_kernel(me_ref, g_ref, h_ref, m1_ref, m2_ref, w_ref, m1_out, m2_out, w_out, *, blocks, tok):
    acc = jnp.zeros(m1_ref.shape, jnp.float32)
    for b in range(blocks):
        part = jnp.dot(
            g_ref[:, b * tok : (b + 1) * tok],
            h_ref[b * tok : (b + 1) * tok, :],
            preferred_element_type=jnp.float32,
        )
        acc = acc + part.astype(jnp.bfloat16).astype(jnp.float32)
    moment_one = beta_one * m1_ref[...] + (1.0 - beta_one) * acc
    moment_two = beta_two * m2_ref[...] + (1.0 - beta_two) * acc * acc
    corrected_one = moment_one / (1.0 - beta_one**STEP)
    corrected_two = moment_two / (1.0 - beta_two**STEP)
    old = w_ref[...].astype(jnp.float32)
    w_out[...] = (
        old - learn_rate * (corrected_one / (jnp.sqrt(corrected_two) + epsilon) + decay_rate * old)
    ).astype(jnp.bfloat16)
    m1_out[...] = moment_one
    m2_out[...] = moment_two


def owner_update(me, grad_rows, hidden_all, first_moment, second_moment, down_weight, tok):
    rows, width = first_moment.shape
    tokens = hidden_all.shape[0]
    tn = 512 if width % 512 == 0 else 256
    grid_spec = pltpu.PrefetchScalarGridSpec(
        num_scalar_prefetch=1,
        grid=(width // tn,),
        in_specs=[
            pl.BlockSpec((rows, tokens), lambda n, me: (0, 0)),
            pl.BlockSpec((tokens, tn), lambda n, me: (0, n)),
            pl.BlockSpec((rows, tn), lambda n, me: (0, n)),
            pl.BlockSpec((rows, tn), lambda n, me: (0, n)),
            pl.BlockSpec((rows, tn), lambda n, me: (me[0], n)),
        ],
        out_specs=[
            pl.BlockSpec((rows, tn), lambda n, me: (0, n)),
            pl.BlockSpec((rows, tn), lambda n, me: (0, n)),
            pl.BlockSpec((rows, tn), lambda n, me: (0, n)),
        ],
    )
    flops = 2 * rows * tokens * width
    nbytes = 2 * rows * tokens + 2 * tokens * width + 16 * rows * width + 4 * rows * width
    return pl.pallas_call(
        functools.partial(adam_kernel, blocks=tokens // tok, tok=tok),
        grid_spec=grid_spec,
        out_shape=[
            jax.ShapeDtypeStruct((rows, width), jnp.float32),
            jax.ShapeDtypeStruct((rows, width), jnp.float32),
            jax.ShapeDtypeStruct((rows, width), jnp.bfloat16),
        ],
        compiler_params=pltpu.CompilerParams(vmem_limit_bytes=48 * 1024 * 1024),
        cost_estimate=pl.CostEstimate(flops=flops, transcendentals=rows * width, bytes_accessed=nbytes),
    )(jnp.reshape(me, (1,)).astype(jnp.int32), grad_rows, hidden_all, first_moment, second_moment, down_weight)


def gather_plane(x, me):
    rows = x.shape[0]
    half = rows // 2

    def swap(v, k):
        return lax.ppermute(v, "dp", [(i, i ^ k) for i in range(8)])

    along_x = swap(x, 2)
    along_y = swap(x, 4)
    partner = swap(x, 1)
    diagonal = jnp.concatenate([swap(along_x[:half], 4), swap(along_y[half:], 2)], axis=0)
    blocks = [
        x,
        partner,
        along_x,
        swap(along_x, 1),
        along_y,
        swap(along_y, 1),
        diagonal,
        swap(diagonal, 1),
    ]
    out = jnp.zeros((8 * rows,) + x.shape[1:], x.dtype)
    for p, block in enumerate(blocks):
        out = lax.dynamic_update_slice_in_dim(out, block, (me ^ p) * rows, 0)
    return out


def shards(grad_out, gate_input, up_input, next_hidden, down_weight, first_moment, second_moment):
    n_dp = lax.axis_size("dp")
    n_t = lax.axis_size("tensor")
    me = lax.axis_index("dp")
    col = lax.axis_index("tensor")
    tok = grad_out.shape[0]
    owned_rows = first_moment.shape[0]
    group = n_dp // n_t

    gate_value = gate_input.astype(jnp.float32)
    up_value = up_input.astype(jnp.float32)
    sigmoid_gate = jax.nn.sigmoid(gate_value)
    activated = gate_value * sigmoid_gate
    hidden = (activated * up_value).astype(jnp.bfloat16)
    hidden, gate_input, up_input = lax.optimization_barrier((hidden, gate_input, up_input))
    gate_value = gate_input.astype(jnp.float32)
    up_value = up_input.astype(jnp.float32)
    sigmoid_gate = jax.nn.sigmoid(gate_value)
    activated = gate_value * sigmoid_gate

    plane = n_dp == 8
    if plane:
        hidden_all = gather_plane(hidden, me)
    else:
        hidden_all = lax.all_gather(hidden, "dp", axis=0, tiled=True)
    next_own, hidden_all = lax.optimization_barrier((next_hidden, hidden_all))
    if plane:
        next_all = gather_plane(next_own, me)
    else:
        next_all = lax.all_gather(next_own, "dp", axis=0, tiled=True)
    grad_rows = lax.all_to_all(grad_out.T, "dp", 0, 1, tiled=True)

    grad_hidden = jnp.dot(grad_out, down_weight, preferred_element_type=jnp.float32)
    gate_grad = (
        grad_hidden * up_value * sigmoid_gate * (1.0 + gate_value * (1.0 - sigmoid_gate))
    ).astype(jnp.bfloat16)
    up_grad = (grad_hidden * activated).astype(jnp.bfloat16)

    moment_one, moment_two, new_shard = owner_update(
        me, grad_rows, hidden_all, first_moment, second_moment, down_weight, tok
    )
    gate_grad, up_grad, new_shard = lax.optimization_barrier((gate_grad, up_grad, new_shard))

    partial_out = lax.dot_general(
        new_shard, next_all, (((1,), (1,)), ((), ())), preferred_element_type=jnp.float32
    )
    summed = (
        lax.psum_scatter(partial_out, "tensor", scatter_dimension=1, tiled=True)
        .astype(jnp.bfloat16)
        .T
    )

    sub = me % group
    pieces = []
    for k in range(group):
        s = (sub + k) % group
        piece = lax.dynamic_slice_in_dim(summed, s * tok, tok, 0)
        perm = []
        for i in range(n_dp):
            for j in range(n_t):
                si = (i % group + k) % group
                dst = (group * j + si) * n_t + i // group
                perm.append((i * n_t + j, dst))
        pieces.append(lax.ppermute(piece, ("dp", "tensor"), perm))
    ordered = []
    for r in range(group):
        chosen = pieces[0]
        for k in range(1, group):
            chosen = jnp.where((sub - k) % group == r, pieces[k], chosen)
        ordered.append(chosen)
    next_out = jnp.concatenate(ordered, axis=1)
    return (gate_grad, up_grad, moment_one, moment_two, next_out)


def solution(mesh):
    n_dp = mesh.shape["dp"]
    n_t = mesh.shape["tensor"]
    if n_dp % n_t:
        raise ValueError("bad mesh")
    placed = (
        P("dp", None),
        P("dp", "tensor"),
        P("dp", "tensor"),
        P("dp", "tensor"),
        P(None, "tensor"),
        P("dp", "tensor"),
        P("dp", "tensor"),
    )
    return jax.shard_map(
        shards,
        mesh=mesh,
        in_specs=placed,
        out_specs=(
            P("dp", "tensor"),
            P("dp", "tensor"),
            P("dp", "tensor"),
            P("dp", "tensor"),
            P("dp", "tensor"),
        ),
        check_vma=False,
    )
```

```python
import functools

import jax
import jax.numpy as jnp
from jax import lax
from jax.experimental import pallas as pl
from jax.experimental.pallas import tpu as pltpu
from jax.sharding import PartitionSpec as P

STEP = 20


beta_one = 0.9
beta_two = 0.95
learn_rate = 0.001
decay_rate = 0.1
epsilon = 1e-08


def adam_kernel(me_ref, g_ref, h_ref, m1_ref, m2_ref, w_ref, m1_out, m2_out, w_out, *, blocks, tok):
    acc = jnp.zeros(m1_ref.shape, jnp.float32)
    for b in range(blocks):
        part = jnp.dot(
            g_ref[:, b * tok : (b + 1) * tok],
            h_ref[b * tok : (b + 1) * tok, :],
            preferred_element_type=jnp.float32,
        )
        acc = acc + part.astype(jnp.bfloat16).astype(jnp.float32)
    moment_one = beta_one * m1_ref[...] + (1.0 - beta_one) * acc
    moment_two = beta_two * m2_ref[...] + (1.0 - beta_two) * acc * acc
    corrected_one = moment_one / (1.0 - beta_one**STEP)
    corrected_two = moment_two / (1.0 - beta_two**STEP)
    old = w_ref[...].astype(jnp.float32)
    w_out[...] = (
        old - learn_rate * (corrected_one / (jnp.sqrt(corrected_two) + epsilon) + decay_rate * old)
    ).astype(jnp.bfloat16)
    m1_out[...] = moment_one
    m2_out[...] = moment_two


def owner_update(me, grad_rows, hidden_all, first_moment, second_moment, down_weight, tok):
    rows, width = first_moment.shape
    tokens = hidden_all.shape[0]
    tn = 512 if width % 512 == 0 else 256
    grid_spec = pltpu.PrefetchScalarGridSpec(
        num_scalar_prefetch=1,
        grid=(width // tn,),
        in_specs=[
            pl.BlockSpec((rows, tokens), lambda n, me: (0, 0)),
            pl.BlockSpec((tokens, tn), lambda n, me: (0, n)),
            pl.BlockSpec((rows, tn), lambda n, me: (0, n)),
            pl.BlockSpec((rows, tn), lambda n, me: (0, n)),
            pl.BlockSpec((rows, tn), lambda n, me: (me[0], n)),
        ],
        out_specs=[
            pl.BlockSpec((rows, tn), lambda n, me: (0, n)),
            pl.BlockSpec((rows, tn), lambda n, me: (0, n)),
            pl.BlockSpec((rows, tn), lambda n, me: (0, n)),
        ],
    )
    flops = 2 * rows * tokens * width
    nbytes = 2 * rows * tokens + 2 * tokens * width + 16 * rows * width + 4 * rows * width
    return pl.pallas_call(
        functools.partial(adam_kernel, blocks=tokens // tok, tok=tok),
        grid_spec=grid_spec,
        out_shape=[
            jax.ShapeDtypeStruct((rows, width), jnp.float32),
            jax.ShapeDtypeStruct((rows, width), jnp.float32),
            jax.ShapeDtypeStruct((rows, width), jnp.bfloat16),
        ],
        compiler_params=pltpu.CompilerParams(vmem_limit_bytes=48 * 1024 * 1024),
        cost_estimate=pl.CostEstimate(flops=flops, transcendentals=rows * width, bytes_accessed=nbytes),
    )(jnp.reshape(me, (1,)).astype(jnp.int32), grad_rows, hidden_all, first_moment, second_moment, down_weight)


def gather_plane(x):
    half = x.shape[0] // 2

    def swap(v, k):
        return lax.ppermute(v, "dp", [(i, i ^ k) for i in range(8)])

    along_x = swap(x, 2)
    along_y = swap(x, 4)
    partner = swap(x, 1)
    diagonal = jnp.concatenate([swap(along_x[:half], 4), swap(along_y[half:], 2)], axis=0)
    blocks = [
        x,
        partner,
        along_x,
        swap(along_x, 1),
        along_y,
        swap(along_y, 1),
        diagonal,
        swap(diagonal, 1),
    ]
    return blocks


def shards(grad_out, gate_input, up_input, next_hidden, down_weight, first_moment, second_moment):
    n_dp = lax.axis_size("dp")
    n_t = lax.axis_size("tensor")
    me = lax.axis_index("dp")
    col = lax.axis_index("tensor")
    tok = grad_out.shape[0]
    owned_rows = first_moment.shape[0]
    group = n_dp // n_t

    gate_value = gate_input.astype(jnp.float32)
    up_value = up_input.astype(jnp.float32)
    sigmoid_gate = jax.nn.sigmoid(gate_value)
    activated = gate_value * sigmoid_gate
    hidden = (activated * up_value).astype(jnp.bfloat16)
    hidden, gate_input, up_input = lax.optimization_barrier((hidden, gate_input, up_input))
    gate_value = gate_input.astype(jnp.float32)
    up_value = up_input.astype(jnp.float32)
    sigmoid_gate = jax.nn.sigmoid(gate_value)
    activated = gate_value * sigmoid_gate

    half = tok // 2
    plane = n_dp == 8
    if plane:
        hidden_blocks = gather_plane(hidden)
    else:
        hidden_blocks = [lax.all_gather(hidden, "dp", axis=0, tiled=True)]
    first_own, hidden_blocks = lax.optimization_barrier((next_hidden[:half], hidden_blocks))
    hidden_all = jnp.concatenate(hidden_blocks, axis=0)
    first_next = lax.all_gather(first_own, "dp", axis=0, tiled=True)
    grad_rows = lax.all_to_all(grad_out.T, "dp", 0, 1, tiled=True)
    if plane:
        grad_rows = jnp.concatenate(
            [lax.dynamic_slice_in_dim(grad_rows, (me ^ p) * tok, tok, 1) for p in range(n_dp)],
            axis=1,
        )

    grad_hidden = jnp.dot(grad_out, down_weight, preferred_element_type=jnp.float32)
    gate_grad = (
        grad_hidden * up_value * sigmoid_gate * (1.0 + gate_value * (1.0 - sigmoid_gate))
    ).astype(jnp.bfloat16)
    up_grad = (grad_hidden * activated).astype(jnp.bfloat16)

    moment_one, moment_two, new_shard = owner_update(
        me, grad_rows, hidden_all, first_moment, second_moment, down_weight, tok
    )
    gate_grad, up_grad, new_shard = lax.optimization_barrier((gate_grad, up_grad, new_shard))

    width = n_dp * half // n_t
    summed_parts = []
    next_part = first_next
    for c in range(2):
        partial_out = lax.dot_general(
            new_shard, next_part, (((1,), (1,)), ((), ())), preferred_element_type=jnp.float32
        )
        if c == 0:
            second_own, partial_out = lax.optimization_barrier((next_hidden[half:], partial_out))
            next_part = lax.all_gather(second_own, "dp", axis=0, tiled=True)
            blocks = lax.all_to_all(partial_out, "tensor", 1, 0, tiled=True)
            blocks, next_part = lax.optimization_barrier((blocks, next_part))
            total = jnp.sum(jnp.reshape(blocks, (n_t,) + partial_out.shape[:1] + (width,)), axis=0)
        else:
            total = lax.psum_scatter(partial_out, "tensor", scatter_dimension=1, tiled=True)
        summed_parts.append(total.astype(jnp.bfloat16).T)

    sub = me % group
    halves = []
    for c in range(2):
        pieces = []
        for k in range(group):
            s = (sub + k) % group
            piece = lax.dynamic_slice_in_dim(summed_parts[c], s * half, half, 0)
            perm = []
            for i in range(n_dp):
                for j in range(n_t):
                    si = (i % group + k) % group
                    dst = (group * j + si) * n_t + i // group
                    perm.append((i * n_t + j, dst))
            pieces.append(lax.ppermute(piece, ("dp", "tensor"), perm))
        ordered = []
        for r in range(group):
            chosen = pieces[0]
            for k in range(1, group):
                chosen = jnp.where((sub - k) % group == r, pieces[k], chosen)
            ordered.append(chosen)
        halves.append(jnp.concatenate(ordered, axis=1))
    next_out = jnp.concatenate(halves, axis=0)
    return (gate_grad, up_grad, moment_one, moment_two, next_out)


def solution(mesh):
    n_dp = mesh.shape["dp"]
    n_t = mesh.shape["tensor"]
    if n_dp % n_t:
        raise ValueError("bad mesh")
    placed = (
        P("dp", None),
        P("dp", "tensor"),
        P("dp", "tensor"),
        P("dp", "tensor"),
        P(None, "tensor"),
        P("dp", "tensor"),
        P("dp", "tensor"),
    )
    return jax.shard_map(
        shards,
        mesh=mesh,
        in_specs=placed,
        out_specs=(
            P("dp", "tensor"),
            P("dp", "tensor"),
            P("dp", "tensor"),
            P("dp", "tensor"),
            P("dp", "tensor"),
        ),
        check_vma=False,
    )
```

```python
import functools

import jax
import jax.numpy as jnp
from jax import lax
from jax.experimental import pallas as pl
from jax.experimental.pallas import tpu as pltpu
from jax.sharding import PartitionSpec as P

STEP = 20


beta_one = 0.9
beta_two = 0.95
learn_rate = 0.001
decay_rate = 0.1
epsilon = 1e-08


def adam_kernel(me_ref, g_ref, h_ref, m1_ref, m2_ref, w_ref, m1_out, m2_out, w_out, *, blocks, tok):
    acc = jnp.zeros(m1_ref.shape, jnp.float32)
    for b in range(blocks):
        part = jnp.dot(
            g_ref[:, b * tok : (b + 1) * tok],
            h_ref[b * tok : (b + 1) * tok, :],
            preferred_element_type=jnp.float32,
        )
        acc = acc + part.astype(jnp.bfloat16).astype(jnp.float32)
    moment_one = beta_one * m1_ref[...] + (1.0 - beta_one) * acc
    moment_two = beta_two * m2_ref[...] + (1.0 - beta_two) * acc * acc
    corrected_one = moment_one / (1.0 - beta_one**STEP)
    corrected_two = moment_two / (1.0 - beta_two**STEP)
    old = w_ref[...].astype(jnp.float32)
    w_out[...] = (
        old - learn_rate * (corrected_one / (jnp.sqrt(corrected_two) + epsilon) + decay_rate * old)
    ).astype(jnp.bfloat16)
    m1_out[...] = moment_one
    m2_out[...] = moment_two


def owner_update(me, grad_rows, hidden_all, first_moment, second_moment, down_weight, tok):
    rows, width = first_moment.shape
    tokens = hidden_all.shape[0]
    tn = 512 if width % 512 == 0 else 256
    grid_spec = pltpu.PrefetchScalarGridSpec(
        num_scalar_prefetch=1,
        grid=(width // tn,),
        in_specs=[
            pl.BlockSpec((rows, tokens), lambda n, me: (0, 0)),
            pl.BlockSpec((tokens, tn), lambda n, me: (0, n)),
            pl.BlockSpec((rows, tn), lambda n, me: (0, n)),
            pl.BlockSpec((rows, tn), lambda n, me: (0, n)),
            pl.BlockSpec((rows, tn), lambda n, me: (me[0], n)),
        ],
        out_specs=[
            pl.BlockSpec((rows, tn), lambda n, me: (0, n)),
            pl.BlockSpec((rows, tn), lambda n, me: (0, n)),
            pl.BlockSpec((rows, tn), lambda n, me: (0, n)),
        ],
    )
    flops = 2 * rows * tokens * width
    nbytes = 2 * rows * tokens + 2 * tokens * width + 16 * rows * width + 4 * rows * width
    return pl.pallas_call(
        functools.partial(adam_kernel, blocks=tokens // tok, tok=tok),
        grid_spec=grid_spec,
        out_shape=[
            jax.ShapeDtypeStruct((rows, width), jnp.float32),
            jax.ShapeDtypeStruct((rows, width), jnp.float32),
            jax.ShapeDtypeStruct((rows, width), jnp.bfloat16),
        ],
        compiler_params=pltpu.CompilerParams(vmem_limit_bytes=48 * 1024 * 1024),
        cost_estimate=pl.CostEstimate(flops=flops, transcendentals=rows * width, bytes_accessed=nbytes),
    )(jnp.reshape(me, (1,)).astype(jnp.int32), grad_rows, hidden_all, first_moment, second_moment, down_weight)


def gather_plane(x):
    half = x.shape[0] // 2

    def swap(v, k):
        return lax.ppermute(v, "dp", [(i, i ^ k) for i in range(8)])

    along_x = swap(x, 2)
    along_y = swap(x, 4)
    partner = swap(x, 1)
    diagonal = jnp.concatenate([swap(along_x[:half], 4), swap(along_y[half:], 2)], axis=0)
    blocks = [
        x,
        partner,
        along_x,
        swap(along_x, 1),
        along_y,
        swap(along_y, 1),
        diagonal,
        swap(diagonal, 1),
    ]
    return blocks


def shards(grad_out, gate_input, up_input, next_hidden, down_weight, first_moment, second_moment):
    n_dp = lax.axis_size("dp")
    n_t = lax.axis_size("tensor")
    me = lax.axis_index("dp")
    col = lax.axis_index("tensor")
    tok = grad_out.shape[0]
    owned_rows = first_moment.shape[0]
    group = n_dp // n_t

    gate_value = gate_input.astype(jnp.float32)
    up_value = up_input.astype(jnp.float32)
    sigmoid_gate = jax.nn.sigmoid(gate_value)
    activated = gate_value * sigmoid_gate
    hidden = (activated * up_value).astype(jnp.bfloat16)
    hidden, gate_input, up_input = lax.optimization_barrier((hidden, gate_input, up_input))
    gate_value = gate_input.astype(jnp.float32)
    up_value = up_input.astype(jnp.float32)
    sigmoid_gate = jax.nn.sigmoid(gate_value)
    activated = gate_value * sigmoid_gate

    half = tok // 2
    plane = n_dp == 8
    if plane:
        hidden_all = jnp.concatenate(gather_plane(hidden), axis=0)
    else:
        hidden_all = lax.all_gather(hidden, "dp", axis=0, tiled=True)
    first_own, hidden_all = lax.optimization_barrier((next_hidden[:half], hidden_all))
    if plane:
        first_next = jnp.concatenate(gather_plane(first_own), axis=0)
    else:
        first_next = lax.all_gather(first_own, "dp", axis=0, tiled=True)
    grad_rows = lax.all_to_all(grad_out.T, "dp", 0, 1, tiled=True)
    if plane:
        grad_rows = jnp.concatenate(
            [lax.dynamic_slice_in_dim(grad_rows, (me ^ p) * tok, tok, 1) for p in range(n_dp)],
            axis=1,
        )

    grad_hidden = jnp.dot(grad_out, down_weight, preferred_element_type=jnp.float32)
    gate_grad = (
        grad_hidden * up_value * sigmoid_gate * (1.0 + gate_value * (1.0 - sigmoid_gate))
    ).astype(jnp.bfloat16)
    up_grad = (grad_hidden * activated).astype(jnp.bfloat16)

    moment_one, moment_two, new_shard = owner_update(
        me, grad_rows, hidden_all, first_moment, second_moment, down_weight, tok
    )
    gate_grad, up_grad, new_shard = lax.optimization_barrier((gate_grad, up_grad, new_shard))

    width = n_dp * half // n_t
    summed_parts = []
    next_part = first_next
    for c in range(2):
        partial_out = lax.dot_general(
            new_shard, next_part, (((1,), (1,)), ((), ())), preferred_element_type=jnp.float32
        )
        if c == 0:
            second_own, partial_out = lax.optimization_barrier((next_hidden[half:], partial_out))
            next_part = lax.all_gather(second_own, "dp", axis=0, tiled=True)
            blocks = lax.all_to_all(partial_out, "tensor", 1, 0, tiled=True)
            blocks, next_part = lax.optimization_barrier((blocks, next_part))
            total = jnp.sum(jnp.reshape(blocks, (n_t,) + partial_out.shape[:1] + (width,)), axis=0)
        else:
            total = lax.psum_scatter(partial_out, "tensor", scatter_dimension=1, tiled=True)
        summed_parts.append(total.astype(jnp.bfloat16).T)

    sub = me % group
    halves = []
    for c in range(2):
        pieces = []
        for k in range(group):
            perm = []
            if plane and c == 0:
                piece = summed_parts[c][k * half : (k + 1) * half]
                for i in range(n_dp):
                    for j in range(n_t):
                        dst = (i ^ (group * j + k)) * n_t + i // group
                        perm.append((i * n_t + j, dst))
            else:
                s = (sub + k) % group
                piece = lax.dynamic_slice_in_dim(summed_parts[c], s * half, half, 0)
                for i in range(n_dp):
                    for j in range(n_t):
                        si = (i % group + k) % group
                        dst = (group * j + si) * n_t + i // group
                        perm.append((i * n_t + j, dst))
            pieces.append(lax.ppermute(piece, ("dp", "tensor"), perm))
        ordered = []
        for r in range(group):
            chosen = pieces[0]
            for k in range(1, group):
                chosen = jnp.where((sub - k) % group == r, pieces[k], chosen)
            ordered.append(chosen)
        halves.append(jnp.concatenate(ordered, axis=1))
    next_out = jnp.concatenate(halves, axis=0)
    return (gate_grad, up_grad, moment_one, moment_two, next_out)


def solution(mesh):
    n_dp = mesh.shape["dp"]
    n_t = mesh.shape["tensor"]
    if n_dp % n_t:
        raise ValueError("bad mesh")
    placed = (
        P("dp", None),
        P("dp", "tensor"),
        P("dp", "tensor"),
        P("dp", "tensor"),
        P(None, "tensor"),
        P("dp", "tensor"),
        P("dp", "tensor"),
    )
    return jax.shard_map(
        shards,
        mesh=mesh,
        in_specs=placed,
        out_specs=(
            P("dp", "tensor"),
            P("dp", "tensor"),
            P("dp", "tensor"),
            P("dp", "tensor"),
            P("dp", "tensor"),
        ),
        check_vma=False,
    )
```

```python
import functools

import jax
import jax.numpy as jnp
from jax import lax
from jax.experimental import pallas as pl
from jax.experimental.pallas import tpu as pltpu
from jax.sharding import PartitionSpec as P

STEP = 20


beta_one = 0.9
beta_two = 0.95
learn_rate = 0.001
decay_rate = 0.1
epsilon = 1e-08


def adam_kernel(me_ref, g_ref, h_ref, m1_ref, m2_ref, w_ref, m1_out, m2_out, w_out, *, blocks, tok):
    acc = jnp.zeros(m1_ref.shape, jnp.float32)
    for b in range(blocks):
        part = jnp.dot(
            g_ref[:, b * tok : (b + 1) * tok],
            h_ref[b * tok : (b + 1) * tok, :],
            preferred_element_type=jnp.float32,
        )
        acc = acc + part.astype(jnp.bfloat16).astype(jnp.float32)
    moment_one = beta_one * m1_ref[...] + (1.0 - beta_one) * acc
    moment_two = beta_two * m2_ref[...] + (1.0 - beta_two) * acc * acc
    corrected_one = moment_one / (1.0 - beta_one**STEP)
    corrected_two = moment_two / (1.0 - beta_two**STEP)
    old = w_ref[...].astype(jnp.float32)
    w_out[...] = (
        old - learn_rate * (corrected_one / (jnp.sqrt(corrected_two) + epsilon) + decay_rate * old)
    ).astype(jnp.bfloat16)
    m1_out[...] = moment_one
    m2_out[...] = moment_two


def owner_update(me, grad_rows, hidden_all, first_moment, second_moment, down_weight, tok):
    rows, width = first_moment.shape
    tokens = hidden_all.shape[0]
    tn = 512 if width % 512 == 0 else 256
    grid_spec = pltpu.PrefetchScalarGridSpec(
        num_scalar_prefetch=1,
        grid=(width // tn,),
        in_specs=[
            pl.BlockSpec((rows, tokens), lambda n, me: (0, 0)),
            pl.BlockSpec((tokens, tn), lambda n, me: (0, n)),
            pl.BlockSpec((rows, tn), lambda n, me: (0, n)),
            pl.BlockSpec((rows, tn), lambda n, me: (0, n)),
            pl.BlockSpec((rows, tn), lambda n, me: (me[0], n)),
        ],
        out_specs=[
            pl.BlockSpec((rows, tn), lambda n, me: (0, n)),
            pl.BlockSpec((rows, tn), lambda n, me: (0, n)),
            pl.BlockSpec((rows, tn), lambda n, me: (0, n)),
        ],
    )
    flops = 2 * rows * tokens * width
    nbytes = 2 * rows * tokens + 2 * tokens * width + 16 * rows * width + 4 * rows * width
    return pl.pallas_call(
        functools.partial(adam_kernel, blocks=tokens // tok, tok=tok),
        grid_spec=grid_spec,
        out_shape=[
            jax.ShapeDtypeStruct((rows, width), jnp.float32),
            jax.ShapeDtypeStruct((rows, width), jnp.float32),
            jax.ShapeDtypeStruct((rows, width), jnp.bfloat16),
        ],
        compiler_params=pltpu.CompilerParams(vmem_limit_bytes=48 * 1024 * 1024),
        cost_estimate=pl.CostEstimate(flops=flops, transcendentals=rows * width, bytes_accessed=nbytes),
    )(jnp.reshape(me, (1,)).astype(jnp.int32), grad_rows, hidden_all, first_moment, second_moment, down_weight)


def gather_plane(x):
    half = x.shape[0] // 2

    def swap(v, k):
        return lax.ppermute(v, "dp", [(i, i ^ k) for i in range(8)])

    along_x = swap(x, 2)
    along_y = swap(x, 4)
    partner = swap(x, 1)
    diagonal = jnp.concatenate([swap(along_x[:half], 4), swap(along_y[half:], 2)], axis=0)
    blocks = [
        x,
        partner,
        along_x,
        swap(along_x, 1),
        along_y,
        swap(along_y, 1),
        diagonal,
        swap(diagonal, 1),
    ]
    return blocks


def shards(grad_out, gate_input, up_input, next_hidden, down_weight, first_moment, second_moment):
    n_dp = lax.axis_size("dp")
    n_t = lax.axis_size("tensor")
    me = lax.axis_index("dp")
    col = lax.axis_index("tensor")
    tok = grad_out.shape[0]
    owned_rows = first_moment.shape[0]
    group = n_dp // n_t

    gate_value = gate_input.astype(jnp.float32)
    up_value = up_input.astype(jnp.float32)
    sigmoid_gate = jax.nn.sigmoid(gate_value)
    activated = gate_value * sigmoid_gate
    hidden = (activated * up_value).astype(jnp.bfloat16)
    hidden, gate_input, up_input = lax.optimization_barrier((hidden, gate_input, up_input))
    gate_value = gate_input.astype(jnp.float32)
    up_value = up_input.astype(jnp.float32)
    sigmoid_gate = jax.nn.sigmoid(gate_value)
    activated = gate_value * sigmoid_gate

    half = tok // 2
    plane = n_dp == 8
    if plane:
        hidden_all = jnp.concatenate(gather_plane(hidden), axis=0)
    else:
        hidden_all = lax.all_gather(hidden, "dp", axis=0, tiled=True)
    first_own, grad_t, hidden_all = lax.optimization_barrier(
        (next_hidden[:half], grad_out.T, hidden_all)
    )
    if plane:
        first_next = jnp.concatenate(gather_plane(first_own), axis=0)
    else:
        first_next = lax.all_gather(first_own, "dp", axis=0, tiled=True)
    grad_rows = lax.all_to_all(grad_t, "dp", 0, 1, tiled=True)
    if plane:
        grad_rows = jnp.concatenate(
            [lax.dynamic_slice_in_dim(grad_rows, (me ^ p) * tok, tok, 1) for p in range(n_dp)],
            axis=1,
        )

    grad_hidden = jnp.dot(grad_out, down_weight, preferred_element_type=jnp.float32)
    gate_grad = (
        grad_hidden * up_value * sigmoid_gate * (1.0 + gate_value * (1.0 - sigmoid_gate))
    ).astype(jnp.bfloat16)
    up_grad = (grad_hidden * activated).astype(jnp.bfloat16)

    moment_one, moment_two, new_shard = owner_update(
        me, grad_rows, hidden_all, first_moment, second_moment, down_weight, tok
    )
    gate_grad, up_grad, new_shard = lax.optimization_barrier((gate_grad, up_grad, new_shard))

    width = n_dp * half // n_t
    summed_parts = []
    next_part = first_next
    for c in range(2):
        partial_out = lax.dot_general(
            new_shard, next_part, (((1,), (1,)), ((), ())), preferred_element_type=jnp.float32
        )
        if c == 0:
            second_own, partial_out = lax.optimization_barrier((next_hidden[half:], partial_out))
            next_part = lax.all_gather(second_own, "dp", axis=0, tiled=True)
            blocks = lax.all_to_all(partial_out, "tensor", 1, 0, tiled=True)
            blocks, next_part = lax.optimization_barrier((blocks, next_part))
            total = jnp.sum(jnp.reshape(blocks, (n_t,) + partial_out.shape[:1] + (width,)), axis=0)
        else:
            total = lax.psum_scatter(partial_out, "tensor", scatter_dimension=1, tiled=True)
        summed_parts.append(total.astype(jnp.bfloat16).T)

    sub = me % group
    halves = []
    for c in range(2):
        pieces = []
        for k in range(group):
            perm = []
            if plane and c == 0:
                piece = summed_parts[c][k * half : (k + 1) * half]
                for i in range(n_dp):
                    for j in range(n_t):
                        dst = (i ^ (group * j + k)) * n_t + i // group
                        perm.append((i * n_t + j, dst))
            else:
                s = (sub + k) % group
                piece = lax.dynamic_slice_in_dim(summed_parts[c], s * half, half, 0)
                for i in range(n_dp):
                    for j in range(n_t):
                        si = (i % group + k) % group
                        dst = (group * j + si) * n_t + i // group
                        perm.append((i * n_t + j, dst))
            pieces.append(lax.ppermute(piece, ("dp", "tensor"), perm))
        ordered = []
        for r in range(group):
            chosen = pieces[0]
            for k in range(1, group):
                chosen = jnp.where((sub - k) % group == r, pieces[k], chosen)
            ordered.append(chosen)
        halves.append(jnp.concatenate(ordered, axis=1))
    next_out = jnp.concatenate(halves, axis=0)
    return (gate_grad, up_grad, moment_one, moment_two, next_out)


def solution(mesh):
    n_dp = mesh.shape["dp"]
    n_t = mesh.shape["tensor"]
    if n_dp % n_t:
        raise ValueError("bad mesh")
    placed = (
        P("dp", None),
        P("dp", "tensor"),
        P("dp", "tensor"),
        P("dp", "tensor"),
        P(None, "tensor"),
        P("dp", "tensor"),
        P("dp", "tensor"),
    )
    return jax.shard_map(
        shards,
        mesh=mesh,
        in_specs=placed,
        out_specs=(
            P("dp", "tensor"),
            P("dp", "tensor"),
            P("dp", "tensor"),
            P("dp", "tensor"),
            P("dp", "tensor"),
        ),
        check_vma=False,
    )
```

```python
import functools

import jax
import jax.numpy as jnp
from jax import lax
from jax.experimental import pallas as pl
from jax.experimental.pallas import tpu as pltpu
from jax.sharding import PartitionSpec as P

STEP = 20


beta_one = 0.9
beta_two = 0.95
learn_rate = 0.001
decay_rate = 0.1
epsilon = 1e-08


def adam_kernel(me_ref, g_ref, h_ref, m1_ref, m2_ref, w_ref, m1_out, m2_out, w_out, *, blocks, tok):
    acc = jnp.zeros(m1_ref.shape, jnp.float32)
    for b in range(blocks):
        part = jnp.dot(
            g_ref[:, b * tok : (b + 1) * tok],
            h_ref[b * tok : (b + 1) * tok, :],
            preferred_element_type=jnp.float32,
        )
        acc = acc + part.astype(jnp.bfloat16).astype(jnp.float32)
    moment_one = beta_one * m1_ref[...] + (1.0 - beta_one) * acc
    moment_two = beta_two * m2_ref[...] + (1.0 - beta_two) * acc * acc
    corrected_one = moment_one / (1.0 - beta_one**STEP)
    corrected_two = moment_two / (1.0 - beta_two**STEP)
    old = w_ref[...].astype(jnp.float32)
    w_out[...] = (
        old - learn_rate * (corrected_one / (jnp.sqrt(corrected_two) + epsilon) + decay_rate * old)
    ).astype(jnp.bfloat16)
    m1_out[...] = moment_one
    m2_out[...] = moment_two


def owner_update(me, grad_rows, hidden_all, first_moment, second_moment, down_weight, tok):
    rows, width = first_moment.shape
    tokens = hidden_all.shape[0]
    tn = 512 if width % 512 == 0 else 256
    grid_spec = pltpu.PrefetchScalarGridSpec(
        num_scalar_prefetch=1,
        grid=(width // tn,),
        in_specs=[
            pl.BlockSpec((rows, tokens), lambda n, me: (0, 0)),
            pl.BlockSpec((tokens, tn), lambda n, me: (0, n)),
            pl.BlockSpec((rows, tn), lambda n, me: (0, n)),
            pl.BlockSpec((rows, tn), lambda n, me: (0, n)),
            pl.BlockSpec((rows, tn), lambda n, me: (me[0], n)),
        ],
        out_specs=[
            pl.BlockSpec((rows, tn), lambda n, me: (0, n)),
            pl.BlockSpec((rows, tn), lambda n, me: (0, n)),
            pl.BlockSpec((rows, tn), lambda n, me: (0, n)),
        ],
    )
    flops = 2 * rows * tokens * width
    nbytes = 2 * rows * tokens + 2 * tokens * width + 16 * rows * width + 4 * rows * width
    return pl.pallas_call(
        functools.partial(adam_kernel, blocks=tokens // tok, tok=tok),
        grid_spec=grid_spec,
        out_shape=[
            jax.ShapeDtypeStruct((rows, width), jnp.float32),
            jax.ShapeDtypeStruct((rows, width), jnp.float32),
            jax.ShapeDtypeStruct((rows, width), jnp.bfloat16),
        ],
        compiler_params=pltpu.CompilerParams(vmem_limit_bytes=48 * 1024 * 1024),
        cost_estimate=pl.CostEstimate(flops=flops, transcendentals=rows * width, bytes_accessed=nbytes),
    )(jnp.reshape(me, (1,)).astype(jnp.int32), grad_rows, hidden_all, first_moment, second_moment, down_weight)


def gather_plane(x, extra=None):
    half = x.shape[0] // 2

    def swap(v, k):
        return lax.ppermute(v, "dp", [(i, i ^ k) for i in range(8)])

    along_x = swap(x, 2)
    along_y = swap(x, 4)
    partner = swap(x, 1)
    if extra is not None:
        along_x, along_y, partner, extra = lax.optimization_barrier((along_x, along_y, partner, extra))
    diagonal = jnp.concatenate([swap(along_x[:half], 4), swap(along_y[half:], 2)], axis=0)
    blocks = [
        x,
        partner,
        along_x,
        swap(along_x, 1),
        along_y,
        swap(along_y, 1),
        diagonal,
        swap(diagonal, 1),
    ]
    return blocks, extra


def shards(grad_out, gate_input, up_input, next_hidden, down_weight, first_moment, second_moment):
    n_dp = lax.axis_size("dp")
    n_t = lax.axis_size("tensor")
    me = lax.axis_index("dp")
    col = lax.axis_index("tensor")
    tok = grad_out.shape[0]
    owned_rows = first_moment.shape[0]
    group = n_dp // n_t

    gate_value = gate_input.astype(jnp.float32)
    up_value = up_input.astype(jnp.float32)
    sigmoid_gate = jax.nn.sigmoid(gate_value)
    activated = gate_value * sigmoid_gate
    hidden = (activated * up_value).astype(jnp.bfloat16)
    hidden, gate_input, up_input = lax.optimization_barrier((hidden, gate_input, up_input))
    gate_value = gate_input.astype(jnp.float32)
    up_value = up_input.astype(jnp.float32)
    sigmoid_gate = jax.nn.sigmoid(gate_value)
    activated = gate_value * sigmoid_gate

    half = tok // 2
    plane = n_dp == 8
    if plane:
        hidden_blocks, grad_t = gather_plane(hidden, grad_out.T)
        hidden_all = jnp.concatenate(hidden_blocks, axis=0)
    else:
        hidden_all = lax.all_gather(hidden, "dp", axis=0, tiled=True)
        grad_t = grad_out.T
    first_own, hidden_all = lax.optimization_barrier((next_hidden[:half], hidden_all))
    if plane:
        first_next = jnp.concatenate(gather_plane(first_own)[0], axis=0)
    else:
        first_next = lax.all_gather(first_own, "dp", axis=0, tiled=True)
    grad_rows = lax.all_to_all(grad_t, "dp", 0, 1, tiled=True)
    if plane:
        grad_rows = jnp.concatenate(
            [lax.dynamic_slice_in_dim(grad_rows, (me ^ p) * tok, tok, 1) for p in range(n_dp)],
            axis=1,
        )

    grad_hidden = jnp.dot(grad_out, down_weight, preferred_element_type=jnp.float32)
    gate_grad = (
        grad_hidden * up_value * sigmoid_gate * (1.0 + gate_value * (1.0 - sigmoid_gate))
    ).astype(jnp.bfloat16)
    up_grad = (grad_hidden * activated).astype(jnp.bfloat16)

    moment_one, moment_two, new_shard = owner_update(
        me, grad_rows, hidden_all, first_moment, second_moment, down_weight, tok
    )
    gate_grad, up_grad, new_shard = lax.optimization_barrier((gate_grad, up_grad, new_shard))

    width = n_dp * half // n_t
    summed_parts = []
    next_part = first_next
    for c in range(2):
        partial_out = lax.dot_general(
            new_shard, next_part, (((1,), (1,)), ((), ())), preferred_element_type=jnp.float32
        )
        if c == 0:
            second_own, partial_out = lax.optimization_barrier((next_hidden[half:], partial_out))
            next_part = lax.all_gather(second_own, "dp", axis=0, tiled=True)
            blocks = lax.all_to_all(partial_out, "tensor", 1, 0, tiled=True)
            blocks, next_part = lax.optimization_barrier((blocks, next_part))
            total = jnp.sum(jnp.reshape(blocks, (n_t,) + partial_out.shape[:1] + (width,)), axis=0)
        else:
            total = lax.psum_scatter(partial_out, "tensor", scatter_dimension=1, tiled=True)
        summed_parts.append(total.astype(jnp.bfloat16).T)

    sub = me % group
    halves = []
    for c in range(2):
        pieces = []
        for k in range(group):
            perm = []
            if plane and c == 0:
                piece = summed_parts[c][k * half : (k + 1) * half]
                for i in range(n_dp):
                    for j in range(n_t):
                        dst = (i ^ (group * j + k)) * n_t + i // group
                        perm.append((i * n_t + j, dst))
            else:
                s = (sub + k) % group
                piece = lax.dynamic_slice_in_dim(summed_parts[c], s * half, half, 0)
                for i in range(n_dp):
                    for j in range(n_t):
                        si = (i % group + k) % group
                        dst = (group * j + si) * n_t + i // group
                        perm.append((i * n_t + j, dst))
            pieces.append(lax.ppermute(piece, ("dp", "tensor"), perm))
        ordered = []
        for r in range(group):
            chosen = pieces[0]
            for k in range(1, group):
                chosen = jnp.where((sub - k) % group == r, pieces[k], chosen)
            ordered.append(chosen)
        halves.append(jnp.concatenate(ordered, axis=1))
    next_out = jnp.concatenate(halves, axis=0)
    return (gate_grad, up_grad, moment_one, moment_two, next_out)


def solution(mesh):
    n_dp = mesh.shape["dp"]
    n_t = mesh.shape["tensor"]
    if n_dp % n_t:
        raise ValueError("bad mesh")
    placed = (
        P("dp", None),
        P("dp", "tensor"),
        P("dp", "tensor"),
        P("dp", "tensor"),
        P(None, "tensor"),
        P("dp", "tensor"),
        P("dp", "tensor"),
    )
    return jax.shard_map(
        shards,
        mesh=mesh,
        in_specs=placed,
        out_specs=(
            P("dp", "tensor"),
            P("dp", "tensor"),
            P("dp", "tensor"),
            P("dp", "tensor"),
            P("dp", "tensor"),
        ),
        check_vma=False,
    )
```
